128 devices in a mesh: prow: 16 (over y, x_hi, core), pcol: 8 (over x_lo, z).
Axes of the slice: x: 4 (x_hi: 2, x_lo: 2; x = x_hi * 2 + x_lo), y: 4, z: 4, core: 2. Of those that a mesh axis runs over, the one named last changes fastest.
Arguments:
- inverse_block: float32 [3, 16, 256, 6, 8, 256], P(None, 'prow', None, None, 'pcol'), as said below
- panel_first: float32 [3, 16, 256, 512], P(None, 'prow', 'pcol'), may hold values from -0.0546875 to 0.0546875
- panel_second: float32 [3, 16, 256, 512], P(None, 'prow', 'pcol'), may hold values from -0.0546875 to 0.0546875
- diag_first: float32 [512, 512], replicated, may hold values from -6 to 6
- diag_second: float32 [512, 512], replicated, may hold values from -6 to 6
- pattern_first: int32 [48], replicated, may hold values from 0 to 1, as said below
- pattern_second: int32 [48], replicated, may hold values from 0 to 1, as said below
Outputs:
- column_first: float32 [3, 16, 256, 512], P(None, 'prow', 'pcol')
- column_second: float32 [3, 16, 256, 512], P(None, 'prow', 'pcol')
- diagonal_first: float32 [512, 512], replicated
- diagonal_second: float32 [512, 512], replicated
The draws below stay inside these ranges and needn't reach their ends.
Inputs may be any that keep to these rules, and one draw needn't show every extreme that they name: inverse_block is symmetric as a matrix of 12288 rows: its entry (i, j) equals its entry (j, i) exactly. `pattern_first`: at least one entry is 1. `pattern_second`: at least one entry is 1.
All inputs are finite; a program needn't handle non-finite values.
Results may differ from the reference program's by a relative error of at most 0.000071.
Values sent between devices are 32-bit elements; how exact they have to be, the bound alone decides.
No kernel may reach another device: no remote copies, remote signals or barrier semaphores. Data moves between devices by JAX's collectives and lax.ppermute only.
A program may use at most 64 MiB of HBM per device.

```python
import jax
import jax.numpy as jnp
from jax import lax

SB = 256
W = 512
NBR_LOC = 3
PROWS = 16
PCOLS = 8
NB = 48
NBC_LOC = 6


def draw_inverse_block(key, part):
    order_rows = NB * SB
    base = jax.random.normal(key, (order_rows, order_rows), jnp.float32)
    symmetric = (base + base.T) * 0.70710678
    return symmetric.reshape(NBR_LOC, PROWS, SB, NBC_LOC, PCOLS, SB)


def pattern_bits(key):
    bits = jax.random.randint(key, (NB,), 0, 2, jnp.int32)
    place = jax.random.randint(jax.random.fold_in(key, 7), (), 0, NB, jnp.int32)
    return bits.at[place].set(1)


def draw_pattern_first(key, part):
    return pattern_bits(jax.random.fold_in(key, 101))


def draw_pattern_second(key, part):
    return pattern_bits(jax.random.fold_in(key, 202))


def level_of(stream_key, shape, split, low, largest):
    factor_of, own = 1.0, jax.random.fold_in(stream_key, 6)
    for axis_at, parts in split:
        draws = jnp.exp(jax.random.uniform(jax.random.fold_in(own, axis_at), (parts,), jnp.float32, low / len(split), largest / len(split)))
        factor_of = factor_of * jnp.repeat(draws, shape[axis_at] // parts).reshape([-1 if axis == axis_at else 1 for axis in range(len(shape))])
    return factor_of


def normal_values(stream_key, shape, width, reach, split=(), held_as=jnp.bfloat16):
    values = jax.random.normal(stream_key, shape, jnp.float32) * width
    if len(split) > 0:
        values = level_of(stream_key, shape, split, -0.22, 0.18) * values
    return jnp.clip(values, min=-reach, max=reach).astype(held_as)


def setup_inputs(seed: int = 0) -> dict:
    streams_of = jax.random.split(jax.random.key(seed), 8)
    inverse_block = draw_inverse_block(jax.random.fold_in(streams_of[7], 71), 0)
    panel_first = normal_values(streams_of[1], (NBR_LOC, PROWS, SB, W), (NB * SB) ** -0.5, 0.0546875, ((1, 16), (2, 8)), jnp.float32)
    panel_second = normal_values(streams_of[2], (NBR_LOC, PROWS, SB, W), (NB * SB) ** -0.5, 0.0546875, ((1, 16), (2, 8)), jnp.float32)
    diag_first = normal_values(streams_of[3], (W, W), 1.0, 6.0, (), jnp.float32)
    diag_second = normal_values(streams_of[4], (W, W), 1.0, 6.0, (), jnp.float32)
    pattern_first = draw_pattern_first(jax.random.fold_in(streams_of[7], 71), 0)
    pattern_second = draw_pattern_second(jax.random.fold_in(streams_of[7], 71), 0)
    return {"inverse_block": inverse_block, "panel_first": panel_first, "panel_second": panel_second, "diag_first": diag_first, "diag_second": diag_second, "pattern_first": pattern_first, "pattern_second": pattern_second}


def one_column(matrix, panel_part, pattern, diag_term):
    order_rows = NB * SB
    kept_mask = jnp.repeat(pattern.astype(jnp.float32), SB)[:, None]
    kept_panel = panel_part.reshape(order_rows, W) * kept_mask
    product = jnp.dot(matrix, kept_panel, precision=lax.Precision.HIGHEST, preferred_element_type=jnp.float32)
    result = -(product * kept_mask)
    diagonal = diag_term - jnp.dot(kept_panel.T, result, precision=lax.Precision.HIGHEST, preferred_element_type=jnp.float32)
    return result.reshape(NBR_LOC, PROWS, SB, W), diagonal


def reference(inverse_block, panel_first, panel_second, diag_first, diag_second, pattern_first, pattern_second):
    matrix = inverse_block.reshape(NB * SB, NB * SB)
    first_col, first_diag = one_column(matrix, panel_first, pattern_first, diag_first)
    second_col, second_diag = one_column(matrix, panel_second, pattern_second, diag_second)
    return (first_col, second_col, first_diag, second_diag)
```

```python
import jax
import jax.numpy as jnp
from jax import lax
from jax.sharding import PartitionSpec as P

TILE = 128


def pack_upper(d):
    n = d.shape[-1] // TILE
    blocks = [
        d[..., i * TILE:(i + 1) * TILE, j * TILE:(j + 1) * TILE]
        for i in range(n)
        for j in range(i, n)
    ]
    return jnp.stack(blocks, axis=-3)


def unpack_upper(packed, n):
    rows = [[None] * n for _ in range(n)]
    k = 0
    for i in range(n):
        for j in range(i, n):
            blk = packed[..., k, :, :]
            rows[i][j] = blk
            if i != j:
                rows[j][i] = jnp.swapaxes(blk, -1, -2)
            k += 1
    return jnp.concatenate([jnp.concatenate(r, axis=-1) for r in rows], axis=-2)


def body(
    inverse_block, panel_first, panel_second, diag_first, diag_second, pattern_first, pattern_second
):
    row_count = lax.axis_size("prow")
    col_count = lax.axis_size("pcol")
    factor = row_count // col_count
    row_index = lax.axis_index("prow")
    col_index = lax.axis_index("pcol")
    row_blocks = inverse_block.shape[0]
    block_rows = inverse_block.shape[2]
    col_blocks = inverse_block.shape[3]
    slice_rows = panel_first.shape[2]
    width = panel_first.shape[3]
    highest = lax.Precision.HIGHEST
    both = ("prow", "pcol")

    def kept_of(pattern, prow):
        return lax.dynamic_index_in_dim(
            pattern.reshape(row_blocks, row_count), prow, 1, False
        ).astype(jnp.float32)

    own_first = kept_of(pattern_first, row_index)
    own_second = kept_of(pattern_second, row_index)
    x = jnp.concatenate(
        [
            panel_first[:, 0] * own_first[:, None, None],
            panel_second[:, 0] * own_second[:, None, None],
        ],
        axis=-1,
    )

    to_reducer = []
    to_owner = []
    for q in range(row_count):
        for c in range(col_count):
            reducer = (col_count * (q // col_count) + c) * col_count + q % col_count
            to_reducer.append((q * col_count + c, reducer))
            to_owner.append((reducer, q * col_count + c))
    x_at_reducer = lax.ppermute(x, both, to_reducer)

    spread = jnp.broadcast_to(x[None], (col_count,) + x.shape)
    gathered = lax.all_to_all(spread, "pcol", 0, 0, tiled=True)
    matrix = inverse_block.reshape(
        row_blocks, col_count, slice_rows, row_blocks, factor, col_count, slice_rows
    )
    partial = jnp.einsum(
        "ljsmpct,jlsw->pcmtw",
        matrix,
        gathered,
        precision=highest,
        preferred_element_type=jnp.float32,
    )
    chunks = partial.reshape(row_count, row_blocks, slice_rows, 2 * width)
    received = lax.all_to_all(chunks, "prow", 0, 0, tiled=True)
    total = jnp.sum(received, axis=0)

    owner_row = col_index + col_count * (row_index // col_count)
    kept_first = kept_of(pattern_first, owner_row)
    kept_second = kept_of(pattern_second, owner_row)
    column = jnp.concatenate(
        [
            -(total[..., :width] * kept_first[:, None, None]),
            -(total[..., width:] * kept_second[:, None, None]),
        ],
        axis=-1,
    )
    parts = jnp.stack(
        [
            jnp.einsum(
                "lsw,lsv->wv",
                x_at_reducer[..., :width],
                column[..., :width],
                precision=highest,
                preferred_element_type=jnp.float32,
            ),
            jnp.einsum(
                "lsw,lsv->wv",
                x_at_reducer[..., width:],
                column[..., width:],
                precision=highest,
                preferred_element_type=jnp.float32,
            ),
        ]
    )
    column_home = lax.ppermute(column, both, to_owner)
    sums = unpack_upper(lax.psum(pack_upper(parts), both), width // TILE)
    return (
        column_home[:, None, :, :width],
        column_home[:, None, :, width:],
        diag_first - sums[0],
        diag_second - sums[1],
    )


def solution(mesh):
    placed = (
        P(None, "prow", None, None, "pcol", None),
        P(None, "prow", "pcol", None),
        P(None, "prow", "pcol", None),
        P(),
        P(),
        P(),
        P(),
    )
    return jax.shard_map(
        body,
        mesh=mesh,
        in_specs=placed,
        out_specs=(P(None, "prow", "pcol", None), P(None, "prow", "pcol", None), P(), P()),
        check_vma=False,
    )
```

```python
import jax
import jax.numpy as jnp
from jax import lax
from jax.sharding import PartitionSpec as P

TILE = 128


def pack_upper(d):
    n = d.shape[-1] // TILE
    blocks = [
        d[..., i * TILE:(i + 1) * TILE, j * TILE:(j + 1) * TILE]
        for i in range(n)
        for j in range(i, n)
    ]
    return jnp.stack(blocks, axis=-3)


def unpack_upper(packed, n):
    rows = [[None] * n for _ in range(n)]
    k = 0
    for i in range(n):
        for j in range(i, n):
            blk = packed[..., k, :, :]
            rows[i][j] = blk
            if i != j:
                rows[j][i] = jnp.swapaxes(blk, -1, -2)
            k += 1
    return jnp.concatenate([jnp.concatenate(r, axis=-1) for r in rows], axis=-2)


def body(
    inverse_block, panel_first, panel_second, diag_first, diag_second, pattern_first, pattern_second
):
    row_count = lax.axis_size("prow")
    col_count = lax.axis_size("pcol")
    factor = row_count // col_count
    row_index = lax.axis_index("prow")
    col_index = lax.axis_index("pcol")
    row_blocks = inverse_block.shape[0]
    block_rows = inverse_block.shape[2]
    col_blocks = inverse_block.shape[3]
    slice_rows = panel_first.shape[2]
    width = panel_first.shape[3]
    highest = lax.Precision.HIGHEST
    both = ("prow", "pcol")

    def kept_of(pattern, prow):
        return lax.dynamic_index_in_dim(
            pattern.reshape(row_blocks, row_count), prow, 1, False
        ).astype(jnp.float32)

    own_first = kept_of(pattern_first, row_index)
    own_second = kept_of(pattern_second, row_index)
    x = jnp.concatenate(
        [
            panel_first[:, 0] * own_first[:, None, None],
            panel_second[:, 0] * own_second[:, None, None],
        ],
        axis=-1,
    )

    to_reducer = []
    to_owner = []
    for q in range(row_count):
        for c in range(col_count):
            reducer = (col_count * (q // col_count) + c) * col_count + q % col_count
            to_reducer.append((q * col_count + c, reducer))
            to_owner.append((reducer, q * col_count + c))
    x_at_reducer = lax.ppermute(x, both, to_reducer)

    spread = jnp.broadcast_to(
        x[:, None], (row_blocks, col_count, slice_rows, 2 * width)
    ).reshape(row_blocks, block_rows, 2 * width)
    gathered = lax.all_to_all(spread, "pcol", 1, 1, tiled=True)
    matrix = inverse_block.reshape(row_blocks, block_rows, col_blocks, block_rows)
    partial = jnp.einsum(
        "lsmt,lsw->mtw",
        matrix,
        gathered,
        precision=highest,
        preferred_element_type=jnp.float32,
    )
    chunks = partial.reshape(row_blocks, row_count, slice_rows, 2 * width)
    received = lax.all_to_all(chunks, "prow", 1, 1, tiled=True)
    total = jnp.sum(received, axis=1)

    owner_row = col_index + col_count * (row_index // col_count)
    kept_first = kept_of(pattern_first, owner_row)
    kept_second = kept_of(pattern_second, owner_row)
    column = jnp.concatenate(
        [
            -(total[..., :width] * kept_first[:, None, None]),
            -(total[..., width:] * kept_second[:, None, None]),
        ],
        axis=-1,
    )
    parts = jnp.stack(
        [
            jnp.einsum(
                "lsw,lsv->wv",
                x_at_reducer[..., :width],
                column[..., :width],
                precision=highest,
                preferred_element_type=jnp.float32,
            ),
            jnp.einsum(
                "lsw,lsv->wv",
                x_at_reducer[..., width:],
                column[..., width:],
                precision=highest,
                preferred_element_type=jnp.float32,
            ),
        ]
    )
    column_home = lax.ppermute(column, both, to_owner)
    devices = row_count * col_count
    packed = pack_upper(parts)
    flat = packed.reshape(devices, packed.size // devices)
    reduced = jnp.sum(lax.all_to_all(flat, both, 0, 0, tiled=True), axis=0)
    spread_sum = jnp.broadcast_to(reduced[None], flat.shape)
    summed = lax.all_to_all(spread_sum, both, 0, 0, tiled=True).reshape(packed.shape)
    sums = unpack_upper(summed, width // TILE)
    return (
        column_home[:, None, :, :width],
        column_home[:, None, :, width:],
        diag_first - sums[0],
        diag_second - sums[1],
    )


def solution(mesh):
    placed = (
        P(None, "prow", None, None, "pcol", None),
        P(None, "prow", "pcol", None),
        P(None, "prow", "pcol", None),
        P(),
        P(),
        P(),
        P(),
    )
    return jax.shard_map(
        body,
        mesh=mesh,
        in_specs=placed,
        out_specs=(P(None, "prow", "pcol", None), P(None, "prow", "pcol", None), P(), P()),
        check_vma=False,
    )
```

```python
import jax
import jax.numpy as jnp
from jax import lax
from jax.sharding import PartitionSpec as P

TILE = 128
PIECE = 512


def pack_upper(d):
    n = d.shape[-1] // TILE
    blocks = [
        d[..., i * TILE:(i + 1) * TILE, j * TILE:(j + 1) * TILE]
        for i in range(n)
        for j in range(i, n)
    ]
    return jnp.stack(blocks, axis=-3)


def unpack_upper(packed, n):
    rows = [[None] * n for _ in range(n)]
    k = 0
    for i in range(n):
        for j in range(i, n):
            blk = packed[..., k, :, :]
            rows[i][j] = blk
            if i != j:
                rows[j][i] = jnp.swapaxes(blk, -1, -2)
            k += 1
    return jnp.concatenate([jnp.concatenate(r, axis=-1) for r in rows], axis=-2)


def body(
    inverse_block, panel_first, panel_second, diag_first, diag_second, pattern_first, pattern_second
):
    row_count = lax.axis_size("prow")
    col_count = lax.axis_size("pcol")
    factor = row_count // col_count
    row_index = lax.axis_index("prow")
    col_index = lax.axis_index("pcol")
    row_blocks = inverse_block.shape[0]
    block_rows = inverse_block.shape[2]
    col_blocks = inverse_block.shape[3]
    slice_rows = panel_first.shape[2]
    width = panel_first.shape[3]
    highest = lax.Precision.HIGHEST
    both = ("prow", "pcol")

    def kept_of(pattern, prow):
        return lax.dynamic_index_in_dim(
            pattern.reshape(row_blocks, row_count), prow, 1, False
        ).astype(jnp.float32)

    own_first = kept_of(pattern_first, row_index)
    own_second = kept_of(pattern_second, row_index)
    x = jnp.concatenate(
        [
            panel_first[:, 0] * own_first[:, None, None],
            panel_second[:, 0] * own_second[:, None, None],
        ],
        axis=-1,
    )

    to_reducer = []
    to_owner = []
    for q in range(row_count):
        for c in range(col_count):
            reducer = (col_count * (q // col_count) + c) * col_count + q % col_count
            to_reducer.append((q * col_count + c, reducer))
            to_owner.append((reducer, q * col_count + c))
    x_at_reducer = lax.ppermute(x, both, to_reducer)

    matrix = inverse_block.reshape(row_blocks, block_rows, col_blocks, block_rows)

    def reduce_piece(piece):
        spread = jnp.broadcast_to(
            piece[:, None], (row_blocks, col_count) + piece.shape[1:]
        ).reshape(row_blocks, block_rows, piece.shape[-1])
        gathered = lax.all_to_all(spread, "pcol", 1, 1, tiled=True)
        partial = jnp.einsum(
            "lsmt,lsw->mtw",
            matrix,
            gathered,
            precision=highest,
            preferred_element_type=jnp.float32,
        )
        chunks = partial.reshape(row_blocks, row_count, slice_rows, piece.shape[-1])
        received = lax.all_to_all(chunks, "prow", 1, 1, tiled=True)
        return jnp.sum(received, axis=1)

    total = jnp.concatenate(
        [reduce_piece(x[..., k * PIECE:(k + 1) * PIECE]) for k in range(2 * width // PIECE)],
        axis=-1,
    )

    owner_row = col_index + col_count * (row_index // col_count)
    kept_first = kept_of(pattern_first, owner_row)
    kept_second = kept_of(pattern_second, owner_row)
    column = jnp.concatenate(
        [
            -(total[..., :width] * kept_first[:, None, None]),
            -(total[..., width:] * kept_second[:, None, None]),
        ],
        axis=-1,
    )
    parts = jnp.stack(
        [
            jnp.einsum(
                "lsw,lsv->wv",
                x_at_reducer[..., :width],
                column[..., :width],
                precision=highest,
                preferred_element_type=jnp.float32,
            ),
            jnp.einsum(
                "lsw,lsv->wv",
                x_at_reducer[..., width:],
                column[..., width:],
                precision=highest,
                preferred_element_type=jnp.float32,
            ),
        ]
    )
    column_home = lax.ppermute(column, both, to_owner)
    devices = row_count * col_count
    packed = pack_upper(parts)
    flat = packed.reshape(devices, packed.size // devices)
    reduced = jnp.sum(lax.all_to_all(flat, both, 0, 0, tiled=True), axis=0)
    spread_sum = jnp.broadcast_to(reduced[None], flat.shape)
    summed = lax.all_to_all(spread_sum, both, 0, 0, tiled=True).reshape(packed.shape)
    sums = unpack_upper(summed, width // TILE)
    return (
        column_home[:, None, :, :width],
        column_home[:, None, :, width:],
        diag_first - sums[0],
        diag_second - sums[1],
    )


def solution(mesh):
    placed = (
        P(None, "prow", None, None, "pcol", None),
        P(None, "prow", "pcol", None),
        P(None, "prow", "pcol", None),
        P(),
        P(),
        P(),
        P(),
    )
    return jax.shard_map(
        body,
        mesh=mesh,
        in_specs=placed,
        out_specs=(P(None, "prow", "pcol", None), P(None, "prow", "pcol", None), P(), P()),
        check_vma=False,
    )
```

```python
import jax
import jax.numpy as jnp
from jax import lax
from jax.sharding import PartitionSpec as P

TILE = 128
PIECE = 512


def pack_upper(d):
    n = d.shape[-1] // TILE
    blocks = [
        d[..., i * TILE:(i + 1) * TILE, j * TILE:(j + 1) * TILE]
        for i in range(n)
        for j in range(i, n)
    ]
    return jnp.stack(blocks, axis=-3)


def unpack_upper(packed, n):
    rows = [[None] * n for _ in range(n)]
    k = 0
    for i in range(n):
        for j in range(i, n):
            blk = packed[..., k, :, :]
            rows[i][j] = blk
            if i != j:
                rows[j][i] = jnp.swapaxes(blk, -1, -2)
            k += 1
    return jnp.concatenate([jnp.concatenate(r, axis=-1) for r in rows], axis=-2)


def body(
    inverse_block, panel_first, panel_second, diag_first, diag_second, pattern_first, pattern_second
):
    prow = ("prow_hi", "core")
    row_count = lax.axis_size(prow)
    pair = lax.axis_size("core")
    core = lax.axis_index("core")
    col_count = lax.axis_size("pcol")
    factor = row_count // col_count
    row_index = lax.axis_index(prow)
    col_index = lax.axis_index("pcol")
    row_blocks = inverse_block.shape[0]
    block_rows = inverse_block.shape[2]
    col_blocks = inverse_block.shape[3]
    slice_rows = panel_first.shape[2]
    width = panel_first.shape[3]
    highest = lax.Precision.HIGHEST
    both = ("prow_hi", "core", "pcol")
    swap = [(b, (b + 1) % pair) for b in range(pair)]

    def pair_sum(value, axis):
        split = value.reshape(value.shape[:axis] + (value.shape[axis] // pair, pair) + value.shape[axis + 1:])
        mine = lax.dynamic_index_in_dim(split, core, axis + 1, False)
        other = lax.dynamic_index_in_dim(split, (core + 1) % pair, axis + 1, False)
        return mine + lax.ppermute(other, "core", swap)

    def kept_of(pattern, prow):
        return lax.dynamic_index_in_dim(
            pattern.reshape(row_blocks, row_count), prow, 1, False
        ).astype(jnp.float32)

    own_first = kept_of(pattern_first, row_index)
    own_second = kept_of(pattern_second, row_index)
    x = jnp.concatenate(
        [
            panel_first[:, 0] * own_first[:, None, None],
            panel_second[:, 0] * own_second[:, None, None],
        ],
        axis=-1,
    )

    to_reducer = []
    to_owner = []
    for q in range(row_count):
        for c in range(col_count):
            reducer = (col_count * (q // col_count) + c) * col_count + q % col_count
            to_reducer.append((q * col_count + c, reducer))
            to_owner.append((reducer, q * col_count + c))
    x_at_reducer = lax.ppermute(x, both, to_reducer)

    matrix = inverse_block.reshape(row_blocks, block_rows, col_blocks, block_rows)

    def reduce_piece(piece):
        spread = jnp.broadcast_to(
            piece[:, None], (row_blocks, col_count) + piece.shape[1:]
        ).reshape(row_blocks, block_rows, piece.shape[-1])
        gathered = lax.all_to_all(spread, "pcol", 1, 1, tiled=True)
        partial = jnp.einsum(
            "lsmt,lsw->mtw",
            matrix,
            gathered,
            precision=highest,
            preferred_element_type=jnp.float32,
        )
        chunks = partial.reshape(row_blocks, row_count, slice_rows, piece.shape[-1])
        received = lax.all_to_all(pair_sum(chunks, 1), "prow_hi", 1, 1, tiled=True)
        return jnp.sum(received, axis=1)

    total = jnp.concatenate(
        [reduce_piece(x[..., k * PIECE:(k + 1) * PIECE]) for k in range(2 * width // PIECE)],
        axis=-1,
    )

    owner_row = col_index + col_count * (row_index // col_count)
    kept_first = kept_of(pattern_first, owner_row)
    kept_second = kept_of(pattern_second, owner_row)
    column = jnp.concatenate(
        [
            -(total[..., :width] * kept_first[:, None, None]),
            -(total[..., width:] * kept_second[:, None, None]),
        ],
        axis=-1,
    )
    parts = jnp.stack(
        [
            jnp.einsum(
                "lsw,lsv->wv",
                x_at_reducer[..., :width],
                column[..., :width],
                precision=highest,
                preferred_element_type=jnp.float32,
            ),
            jnp.einsum(
                "lsw,lsv->wv",
                x_at_reducer[..., width:],
                column[..., width:],
                precision=highest,
                preferred_element_type=jnp.float32,
            ),
        ]
    )
    column_home = lax.ppermute(column, both, to_owner)
    packed = pack_upper(parts)
    others = ("prow_hi", "pcol")
    devices = lax.axis_size(others)
    half = pair_sum(packed.reshape(pair * devices, packed.size // (pair * devices)), 0)
    flat = half.reshape(devices, half.size // devices)
    reduced = jnp.sum(lax.all_to_all(flat, others, 0, 0, tiled=True), axis=0)
    spread_sum = jnp.broadcast_to(reduced[None], flat.shape)
    mine = lax.all_to_all(spread_sum, others, 0, 0, tiled=True).reshape(half.shape)
    other = lax.ppermute(mine, "core", swap)
    summed = jnp.where(
        core == 0,
        jnp.stack([mine, other], axis=1),
        jnp.stack([other, mine], axis=1),
    ).reshape(packed.shape)
    sums = unpack_upper(summed, width // TILE)
    return (
        column_home[:, None, :, :width],
        column_home[:, None, :, width:],
        diag_first - sums[0],
        diag_second - sums[1],
    )


def solution(mesh):
    rows, cols = mesh.devices.shape
    split = jax.sharding.Mesh(mesh.devices.reshape(rows // 2, 2, cols), ("prow_hi", "core", "pcol"))
    prow = ("prow_hi", "core")
    placed = (
        P(None, prow, None, None, "pcol", None),
        P(None, prow, "pcol", None),
        P(None, prow, "pcol", None),
        P(),
        P(),
        P(),
        P(),
    )
    return jax.shard_map(
        body,
        mesh=split,
        in_specs=placed,
        out_specs=(P(None, prow, "pcol", None), P(None, prow, "pcol", None), P(), P()),
        check_vma=False,
    )
```

```python
import jax
import jax.numpy as jnp
from jax import lax
from jax.sharding import PartitionSpec as P

TILE = 128
PIECE = 512


def pack_upper(d):
    n = d.shape[-1] // TILE
    blocks = [
        d[..., i * TILE:(i + 1) * TILE, j * TILE:(j + 1) * TILE]
        for i in range(n)
        for j in range(i, n)
    ]
    return jnp.stack(blocks, axis=-3)


def unpack_upper(packed, n):
    rows = [[None] * n for _ in range(n)]
    k = 0
    for i in range(n):
        for j in range(i, n):
            blk = packed[..., k, :, :]
            rows[i][j] = blk
            if i != j:
                rows[j][i] = jnp.swapaxes(blk, -1, -2)
            k += 1
    return jnp.concatenate([jnp.concatenate(r, axis=-1) for r in rows], axis=-2)


def body(
    inverse_block, panel_first, panel_second, diag_first, diag_second, pattern_first, pattern_second
):
    prow = ("prow_hi", "core")
    row_count = lax.axis_size(prow)
    pair = lax.axis_size("core")
    core = lax.axis_index("core")
    col_count = lax.axis_size("pcol")
    factor = row_count // col_count
    row_index = lax.axis_index(prow)
    col_index = lax.axis_index("pcol")
    row_blocks = inverse_block.shape[0]
    block_rows = inverse_block.shape[2]
    col_blocks = inverse_block.shape[3]
    slice_rows = panel_first.shape[2]
    width = panel_first.shape[3]
    highest = lax.Precision.HIGHEST
    both = ("prow_hi", "core", "pcol")
    swap = [(b, (b + 1) % pair) for b in range(pair)]

    def pair_sum(value, axis):
        split = value.reshape(value.shape[:axis] + (value.shape[axis] // pair, pair) + value.shape[axis + 1:])
        mine = lax.dynamic_index_in_dim(split, core, axis + 1, False)
        other = lax.dynamic_index_in_dim(split, (core + 1) % pair, axis + 1, False)
        return mine + lax.ppermute(other, "core", swap)

    def kept_of(pattern, prow):
        return lax.dynamic_index_in_dim(
            pattern.reshape(row_blocks, row_count), prow, 1, False
        ).astype(jnp.float32)

    own_first = kept_of(pattern_first, row_index)
    own_second = kept_of(pattern_second, row_index)
    x = jnp.concatenate(
        [
            panel_first[:, 0] * own_first[:, None, None],
            panel_second[:, 0] * own_second[:, None, None],
        ],
        axis=-1,
    )

    to_reducer = []
    to_owner = []
    for q in range(row_count):
        for c in range(col_count):
            reducer = (col_count * (q // col_count) + c) * col_count + q % col_count
            to_reducer.append((q * col_count + c, reducer))
            to_owner.append((reducer, q * col_count + c))
    x_at_reducer = lax.ppermute(x, both, to_reducer)

    matrix = inverse_block.reshape(row_blocks, block_rows, col_blocks, block_rows)

    def reduce_piece(piece, by_permutes):
        if by_permutes:
            held = [None] * col_count
            held[0] = piece
            for k in range(1, col_count):
                held[k] = lax.ppermute(
                    piece, "pcol", [(i, (i + k) % col_count) for i in range(col_count)]
                )
            order = jnp.stack(held, axis=1)
            source = (col_index - jnp.arange(col_count)) % col_count
            slot = jnp.argsort(source)
            gathered = jnp.take(order, slot, axis=1).reshape(row_blocks, block_rows, piece.shape[-1])
        else:
            spread = jnp.broadcast_to(
                piece[:, None], (row_blocks, col_count) + piece.shape[1:]
            ).reshape(row_blocks, block_rows, piece.shape[-1])
            gathered = lax.all_to_all(spread, "pcol", 1, 1, tiled=True)
        partial = jnp.einsum(
            "lsmt,lsw->mtw",
            matrix,
            gathered,
            precision=highest,
            preferred_element_type=jnp.float32,
        )
        chunks = partial.reshape(row_blocks, row_count, slice_rows, piece.shape[-1])
        received = lax.all_to_all(pair_sum(chunks, 1), "prow_hi", 1, 1, tiled=True)
        return jnp.sum(received, axis=1)

    total = jnp.concatenate(
        [
            reduce_piece(x[..., k * PIECE:(k + 1) * PIECE], k > 0)
            for k in range(2 * width // PIECE)
        ],
        axis=-1,
    )

    owner_row = col_index + col_count * (row_index // col_count)
    kept_first = kept_of(pattern_first, owner_row)
    kept_second = kept_of(pattern_second, owner_row)
    column = jnp.concatenate(
        [
            -(total[..., :width] * kept_first[:, None, None]),
            -(total[..., width:] * kept_second[:, None, None]),
        ],
        axis=-1,
    )
    parts = jnp.stack(
        [
            jnp.einsum(
                "lsw,lsv->wv",
                x_at_reducer[..., :width],
                column[..., :width],
                precision=highest,
                preferred_element_type=jnp.float32,
            ),
            jnp.einsum(
                "lsw,lsv->wv",
                x_at_reducer[..., width:],
                column[..., width:],
                precision=highest,
                preferred_element_type=jnp.float32,
            ),
        ]
    )
    column_home = lax.ppermute(column, both, to_owner)
    packed = pack_upper(parts)
    others = ("prow_hi", "pcol")
    devices = lax.axis_size(others)
    half = pair_sum(packed.reshape(pair * devices, packed.size // (pair * devices)), 0)
    flat = half.reshape(devices, half.size // devices)
    reduced = jnp.sum(lax.all_to_all(flat, others, 0, 0, tiled=True), axis=0)
    spread_sum = jnp.broadcast_to(reduced[None], flat.shape)
    mine = lax.all_to_all(spread_sum, others, 0, 0, tiled=True).reshape(half.shape)
    other = lax.ppermute(mine, "core", swap)
    summed = jnp.where(
        core == 0,
        jnp.stack([mine, other], axis=1),
        jnp.stack([other, mine], axis=1),
    ).reshape(packed.shape)
    sums = unpack_upper(summed, width // TILE)
    return (
        column_home[:, None, :, :width],
        column_home[:, None, :, width:],
        diag_first - sums[0],
        diag_second - sums[1],
    )


def solution(mesh):
    rows, cols = mesh.devices.shape
    split = jax.sharding.Mesh(mesh.devices.reshape(rows // 2, 2, cols), ("prow_hi", "core", "pcol"))
    prow = ("prow_hi", "core")
    placed = (
        P(None, prow, None, None, "pcol", None),
        P(None, prow, "pcol", None),
        P(None, prow, "pcol", None),
        P(),
        P(),
        P(),
        P(),
    )
    return jax.shard_map(
        body,
        mesh=split,
        in_specs=placed,
        out_specs=(P(None, prow, "pcol", None), P(None, prow, "pcol", None), P(), P()),
        check_vma=False,
    )
```

```python
import jax
import jax.numpy as jnp
from jax import lax
from jax.sharding import PartitionSpec as P

TILE = 128
PIECE = 512


def pack_upper(d):
    n = d.shape[-1] // TILE
    blocks = [
        d[..., i * TILE:(i + 1) * TILE, j * TILE:(j + 1) * TILE]
        for i in range(n)
        for j in range(i, n)
    ]
    return jnp.stack(blocks, axis=-3)


def unpack_upper(packed, n):
    rows = [[None] * n for _ in range(n)]
    k = 0
    for i in range(n):
        for j in range(i, n):
            blk = packed[..., k, :, :]
            rows[i][j] = blk
            if i != j:
                rows[j][i] = jnp.swapaxes(blk, -1, -2)
            k += 1
    return jnp.concatenate([jnp.concatenate(r, axis=-1) for r in rows], axis=-2)


def body(
    inverse_block, panel_first, panel_second, diag_first, diag_second, pattern_first, pattern_second
):
    prow = ("prow_hi", "core")
    row_count = lax.axis_size(prow)
    pair = lax.axis_size("core")
    core = lax.axis_index("core")
    col_count = lax.axis_size("pcol")
    factor = row_count // col_count
    row_index = lax.axis_index(prow)
    col_index = lax.axis_index("pcol")
    row_blocks = inverse_block.shape[0]
    block_rows = inverse_block.shape[2]
    col_blocks = inverse_block.shape[3]
    slice_rows = panel_first.shape[2]
    width = panel_first.shape[3]
    highest = lax.Precision.HIGHEST
    both = ("prow_hi", "core", "pcol")
    swap = [(b, (b + 1) % pair) for b in range(pair)]

    def pair_sum(value, axis):
        split = value.reshape(value.shape[:axis] + (value.shape[axis] // pair, pair) + value.shape[axis + 1:])
        mine = lax.dynamic_index_in_dim(split, core, axis + 1, False)
        other = lax.dynamic_index_in_dim(split, (core + 1) % pair, axis + 1, False)
        return mine + lax.ppermute(other, "core", swap)

    def kept_of(pattern, prow):
        return lax.dynamic_index_in_dim(
            pattern.reshape(row_blocks, row_count), prow, 1, False
        ).astype(jnp.float32)

    own_first = kept_of(pattern_first, row_index)
    own_second = kept_of(pattern_second, row_index)
    x = jnp.concatenate(
        [
            panel_first[:, 0] * own_first[:, None, None],
            panel_second[:, 0] * own_second[:, None, None],
        ],
        axis=-1,
    )

    to_reducer = []
    to_owner = []
    for q in range(row_count):
        for c in range(col_count):
            reducer = (col_count * (q // col_count) + c) * col_count + q % col_count
            to_reducer.append((q * col_count + c, reducer))
            to_owner.append((reducer, q * col_count + c))
    x_at_reducer = lax.ppermute(x, both, to_reducer)

    matrix = inverse_block.reshape(row_blocks, block_rows, col_blocks, block_rows)

    def reduce_piece(piece, by_permutes):
        if by_permutes:
            held = [None] * col_count
            held[0] = piece
            for k in range(1, col_count):
                held[k] = lax.ppermute(
                    piece, "pcol", [(i, (i + k) % col_count) for i in range(col_count)]
                )
            order = jnp.stack(held, axis=1)
            source = (col_index - jnp.arange(col_count)) % col_count
            slot = jnp.argsort(source)
            gathered = jnp.take(order, slot, axis=1).reshape(row_blocks, block_rows, piece.shape[-1])
        else:
            spread = jnp.broadcast_to(
                piece[:, None], (row_blocks, col_count) + piece.shape[1:]
            ).reshape(row_blocks, block_rows, piece.shape[-1])
            gathered = lax.all_to_all(spread, "pcol", 1, 1, tiled=True)
        partial = jnp.einsum(
            "lsmt,lsw->mtw",
            matrix,
            gathered,
            precision=highest,
            preferred_element_type=jnp.float32,
        )
        chunks = partial.reshape(row_blocks, row_count, slice_rows, piece.shape[-1])
        received = lax.all_to_all(pair_sum(chunks, 1), "prow_hi", 1, 1, tiled=True)
        return jnp.sum(received, axis=1)

    def all_sum(value):
        steps = [("core", 0)]
        for axis, order in (("pcol", (2, 0, 1)), ("prow_hi", (1, 0, 2))):
            bits = lax.axis_size(axis).bit_length() - 1
            steps += [(axis, b) for b in order if b < bits]
        held = value.reshape(-1)
        for axis, b in steps:
            size = lax.axis_size(axis)
            bit = (lax.axis_index(axis) >> b) & 1
            pairs = [(i, i ^ (1 << b)) for i in range(size)]
            halves = held.reshape(2, held.size // 2)
            keep = lax.dynamic_index_in_dim(halves, bit, 0, False)
            send = lax.dynamic_index_in_dim(halves, 1 - bit, 0, False)
            held = keep + lax.ppermute(send, axis, pairs)
        for axis, b in reversed(steps):
            size = lax.axis_size(axis)
            bit = (lax.axis_index(axis) >> b) & 1
            pairs = [(i, i ^ (1 << b)) for i in range(size)]
            got = lax.ppermute(held, axis, pairs)
            held = jnp.where(
                bit == 0,
                jnp.concatenate([held, got]),
                jnp.concatenate([got, held]),
            )
        return held.reshape(value.shape)

    owner_row = col_index + col_count * (row_index // col_count)
    outs = []
    for k, (pattern, diag) in enumerate(
        ((pattern_first, diag_first), (pattern_second, diag_second))
    ):
        lo, hi = k * width, (k + 1) * width
        total = reduce_piece(x[..., lo:hi], k > 0)
        kept = kept_of(pattern, owner_row)
        column = -(total * kept[:, None, None])
        part = jnp.einsum(
            "lsw,lsv->wv",
            x_at_reducer[..., lo:hi],
            column,
            precision=highest,
            preferred_element_type=jnp.float32,
        )
        column_home = lax.ppermute(column, both, to_owner)
        sums = unpack_upper(all_sum(pack_upper(part)), width // TILE)
        outs.append((column_home[:, None], diag - sums))
    return (outs[0][0], outs[1][0], outs[0][1], outs[1][1])


def solution(mesh):
    rows, cols = mesh.devices.shape
    split = jax.sharding.Mesh(mesh.devices.reshape(rows // 2, 2, cols), ("prow_hi", "core", "pcol"))
    prow = ("prow_hi", "core")
    placed = (
        P(None, prow, None, None, "pcol", None),
        P(None, prow, "pcol", None),
        P(None, prow, "pcol", None),
        P(),
        P(),
        P(),
        P(),
    )
    return jax.shard_map(
        body,
        mesh=split,
        in_specs=placed,
        out_specs=(P(None, prow, "pcol", None), P(None, prow, "pcol", None), P(), P()),
        check_vma=False,
    )
```

```python
import jax
import jax.numpy as jnp
from jax import lax
from jax.sharding import PartitionSpec as P

TILE = 128
PIECE = 512


def pack_upper(d):
    n = d.shape[-1] // TILE
    blocks = [
        d[..., i * TILE:(i + 1) * TILE, j * TILE:(j + 1) * TILE]
        for i in range(n)
        for j in range(i, n)
    ]
    return jnp.stack(blocks, axis=-3)


def unpack_upper(packed, n):
    rows = [[None] * n for _ in range(n)]
    k = 0
    for i in range(n):
        for j in range(i, n):
            blk = packed[..., k, :, :]
            rows[i][j] = blk
            if i != j:
                rows[j][i] = jnp.swapaxes(blk, -1, -2)
            k += 1
    return jnp.concatenate([jnp.concatenate(r, axis=-1) for r in rows], axis=-2)


def body(
    inverse_block, panel_first, panel_second, diag_first, diag_second, pattern_first, pattern_second
):
    prow = ("prow_hi", "core")
    row_count = lax.axis_size(prow)
    pair = lax.axis_size("core")
    core = lax.axis_index("core")
    col_count = lax.axis_size("pcol")
    factor = row_count // col_count
    row_index = lax.axis_index(prow)
    col_index = lax.axis_index("pcol")
    row_blocks = inverse_block.shape[0]
    block_rows = inverse_block.shape[2]
    col_blocks = inverse_block.shape[3]
    slice_rows = panel_first.shape[2]
    width = panel_first.shape[3]
    highest = lax.Precision.HIGHEST
    both = ("prow_hi", "core", "pcol")
    swap = [(b, (b + 1) % pair) for b in range(pair)]

    def pair_sum(value, axis):
        split = value.reshape(value.shape[:axis] + (value.shape[axis] // pair, pair) + value.shape[axis + 1:])
        mine = lax.dynamic_index_in_dim(split, core, axis + 1, False)
        other = lax.dynamic_index_in_dim(split, (core + 1) % pair, axis + 1, False)
        return mine + lax.ppermute(other, "core", swap)

    def kept_of(pattern, prow):
        return lax.dynamic_index_in_dim(
            pattern.reshape(row_blocks, row_count), prow, 1, False
        ).astype(jnp.float32)

    own_first = kept_of(pattern_first, row_index)
    own_second = kept_of(pattern_second, row_index)
    x = jnp.concatenate(
        [
            panel_first[:, 0] * own_first[:, None, None],
            panel_second[:, 0] * own_second[:, None, None],
        ],
        axis=-1,
    )

    to_reducer = []
    to_owner = []
    for q in range(row_count):
        for c in range(col_count):
            reducer = (col_count * (q // col_count) + c) * col_count + q % col_count
            to_reducer.append((q * col_count + c, reducer))
            to_owner.append((reducer, q * col_count + c))
    x_at_reducer = lax.ppermute(x, both, to_reducer)

    matrix = inverse_block.reshape(row_blocks, block_rows, col_blocks, block_rows)

    source = (col_index - jnp.arange(col_count)) % col_count
    rotated = jnp.take(
        matrix.reshape(row_blocks, col_count, slice_rows, col_blocks, block_rows),
        source,
        axis=1,
    ).reshape(matrix.shape)

    def reduce_piece(piece):
        held = [piece]
        for k in range(1, col_count):
            held.append(
                lax.ppermute(piece, "pcol", [(i, (i + k) % col_count) for i in range(col_count)])
            )
        gathered = jnp.stack(held, axis=1).reshape(row_blocks, block_rows, piece.shape[-1])
        partial = jnp.einsum(
            "lsmt,lsw->mtw",
            rotated,
            gathered,
            precision=highest,
            preferred_element_type=jnp.float32,
        )
        chunks = partial.reshape(row_blocks, row_count, slice_rows, piece.shape[-1])
        received = lax.all_to_all(pair_sum(chunks, 1), "prow_hi", 1, 1, tiled=True)
        return jnp.sum(received, axis=1)

    total = jnp.concatenate(
        [
            reduce_piece(x[..., k * PIECE:(k + 1) * PIECE])
            for k in range(2 * width // PIECE)
        ],
        axis=-1,
    )

    owner_row = col_index + col_count * (row_index // col_count)
    kept_first = kept_of(pattern_first, owner_row)
    kept_second = kept_of(pattern_second, owner_row)
    column = jnp.concatenate(
        [
            -(total[..., :width] * kept_first[:, None, None]),
            -(total[..., width:] * kept_second[:, None, None]),
        ],
        axis=-1,
    )
    parts = jnp.stack(
        [
            jnp.einsum(
                "lsw,lsv->wv",
                x_at_reducer[..., :width],
                column[..., :width],
                precision=highest,
                preferred_element_type=jnp.float32,
            ),
            jnp.einsum(
                "lsw,lsv->wv",
                x_at_reducer[..., width:],
                column[..., width:],
                precision=highest,
                preferred_element_type=jnp.float32,
            ),
        ]
    )
    column_home = lax.ppermute(column, both, to_owner)
    packed = pack_upper(parts)
    others = ("prow_hi", "pcol")
    devices = lax.axis_size(others)
    half = pair_sum(packed.reshape(pair * devices, packed.size // (pair * devices)), 0)
    flat = half.reshape(devices, half.size // devices)
    reduced = jnp.sum(lax.all_to_all(flat, others, 0, 0, tiled=True), axis=0)
    spread_sum = jnp.broadcast_to(reduced[None], flat.shape)
    mine = lax.all_to_all(spread_sum, others, 0, 0, tiled=True).reshape(half.shape)
    other = lax.ppermute(mine, "core", swap)
    summed = jnp.where(
        core == 0,
        jnp.stack([mine, other], axis=1),
        jnp.stack([other, mine], axis=1),
    ).reshape(packed.shape)
    sums = unpack_upper(summed, width // TILE)
    return (
        column_home[:, None, :, :width],
        column_home[:, None, :, width:],
        diag_first - sums[0],
        diag_second - sums[1],
    )


def solution(mesh):
    rows, cols = mesh.devices.shape
    split = jax.sharding.Mesh(mesh.devices.reshape(rows // 2, 2, cols), ("prow_hi", "core", "pcol"))
    prow = ("prow_hi", "core")
    placed = (
        P(None, prow, None, None, "pcol", None),
        P(None, prow, "pcol", None),
        P(None, prow, "pcol", None),
        P(),
        P(),
        P(),
        P(),
    )
    return jax.shard_map(
        body,
        mesh=split,
        in_specs=placed,
        out_specs=(P(None, prow, "pcol", None), P(None, prow, "pcol", None), P(), P()),
        check_vma=False,
    )
```

```python
import jax
import jax.numpy as jnp
from jax import lax
from jax.sharding import PartitionSpec as P


TILE = 128
PIECE = 512


def pack_upper(d):
    n = d.shape[-1] // TILE
    blocks = [
        d[..., i * TILE:(i + 1) * TILE, j * TILE:(j + 1) * TILE]
        for i in range(n)
        for j in range(i, n)
    ]
    return jnp.stack(blocks, axis=-3)


def unpack_upper(packed, n):
    rows = [[None] * n for _ in range(n)]
    k = 0
    for i in range(n):
        for j in range(i, n):
            blk = packed[..., k, :, :]
            rows[i][j] = blk
            if i != j:
                rows[j][i] = jnp.swapaxes(blk, -1, -2)
            k += 1
    return jnp.concatenate([jnp.concatenate(r, axis=-1) for r in rows], axis=-2)


def body(
    inverse_block, panel_first, panel_second, diag_first, diag_second, pattern_first, pattern_second
):
    prow = ("prow_hi", "core")
    row_count = lax.axis_size(prow)
    pair = lax.axis_size("core")
    core = lax.axis_index("core")
    col_count = lax.axis_size("pcol")
    row_index = lax.axis_index(prow)
    col_index = lax.axis_index("pcol")
    row_blocks = inverse_block.shape[0]
    block_rows = inverse_block.shape[2]
    col_blocks = inverse_block.shape[3]
    slice_rows = panel_first.shape[2]
    width = panel_first.shape[3]
    highest = lax.Precision.HIGHEST
    both = ("prow_hi", "core", "pcol")
    swap = [(b, (b + 1) % pair) for b in range(pair)]

    def pair_sum(value, axis):
        split = value.reshape(value.shape[:axis] + (value.shape[axis] // pair, pair) + value.shape[axis + 1:])
        mine = lax.dynamic_index_in_dim(split, core, axis + 1, False)
        other = lax.dynamic_index_in_dim(split, (core + 1) % pair, axis + 1, False)
        return mine + lax.ppermute(other, "core", swap)

    def kept_of(pattern, prow):
        return lax.dynamic_index_in_dim(
            pattern.reshape(row_blocks, row_count), prow, 1, False
        ).astype(jnp.float32)

    own_first = kept_of(pattern_first, row_index)
    own_second = kept_of(pattern_second, row_index)
    x = jnp.concatenate(
        [
            panel_first[:, 0] * own_first[:, None, None],
            panel_second[:, 0] * own_second[:, None, None],
        ],
        axis=-1,
    )

    to_reducer = []
    to_owner = []
    for q in range(row_count):
        for c in range(col_count):
            reducer = (col_count * (q // col_count) + c) * col_count + q % col_count
            to_reducer.append((q * col_count + c, reducer))
            to_owner.append((reducer, q * col_count + c))
    x_at_reducer = lax.ppermute(x, both, to_reducer)

    matrix = inverse_block.reshape(row_blocks, block_rows, col_blocks, block_rows)

    def reduce_inner(piece, by_permutes):
        gathered = gather_piece(piece, by_permutes)
        return reduce_gathered(piece, gathered)

    def gather_piece(piece, by_permutes):
        if by_permutes:
            held = [None] * col_count
            held[0] = piece
            for k in range(1, col_count):
                held[k] = lax.ppermute(
                    piece, "pcol", [(i, (i + k) % col_count) for i in range(col_count)]
                )
            order = jnp.stack(held, axis=1)
            source = (col_index - jnp.arange(col_count)) % col_count
            slot = jnp.argsort(source)
            gathered = jnp.take(order, slot, axis=1).reshape(row_blocks, block_rows, piece.shape[-1])
        else:
            spread = jnp.broadcast_to(
                piece[:, None], (row_blocks, col_count) + piece.shape[1:]
            ).reshape(row_blocks, block_rows, piece.shape[-1])
            gathered = lax.all_to_all(spread, "pcol", 1, 1, tiled=True)
        return gathered

    def reduce_gathered(piece, gathered):
        partial = jnp.einsum(
            "lsmt,lsw->mtw",
            matrix,
            gathered,
            precision=highest,
            preferred_element_type=jnp.float32,
        )
        chunks = partial.reshape(row_blocks, row_count, slice_rows, piece.shape[-1])
        received = lax.all_to_all(pair_sum(chunks, 1), "prow_hi", 1, 1, tiled=True)
        return jnp.sum(received, axis=1)

    total = jnp.concatenate(
        [reduce_inner(x[..., k * PIECE:(k + 1) * PIECE], k > 0) for k in range(2 * width // PIECE)],
        axis=-1,
    )

    owner_row = col_index + col_count * (row_index // col_count)
    kept_first = kept_of(pattern_first, owner_row)
    kept_second = kept_of(pattern_second, owner_row)
    column = jnp.concatenate(
        [
            -(total[..., :width] * kept_first[:, None, None]),
            -(total[..., width:] * kept_second[:, None, None]),
        ],
        axis=-1,
    )
    parts = jnp.stack(
        [
            jnp.einsum(
                "lsw,lsv->wv",
                x_at_reducer[..., :width],
                column[..., :width],
                precision=highest,
                preferred_element_type=jnp.float32,
            ),
            jnp.einsum(
                "lsw,lsv->wv",
                x_at_reducer[..., width:],
                column[..., width:],
                precision=highest,
                preferred_element_type=jnp.float32,
            ),
        ]
    )
    column_home = lax.ppermute(column, both, to_owner)
    packed = pack_upper(parts)
    others = ("prow_hi", "pcol")
    devices = lax.axis_size(others)
    half = pair_sum(packed.reshape(pair * devices, packed.size // (pair * devices)), 0)
    flat = half.reshape(devices, half.size // devices)
    reduced = jnp.sum(lax.all_to_all(flat, others, 0, 0, tiled=True), axis=0)
    spread_sum = jnp.broadcast_to(reduced[None], flat.shape)
    mine = lax.all_to_all(spread_sum, others, 0, 0, tiled=True).reshape(half.shape)
    other = lax.ppermute(mine, "core", swap)
    summed = jnp.where(
        core == 0,
        jnp.stack([mine, other], axis=1),
        jnp.stack([other, mine], axis=1),
    ).reshape(packed.shape)
    sums = unpack_upper(summed, width // TILE)
    return (
        column_home[:, None, :, :width],
        column_home[:, None, :, width:],
        diag_first - sums[0],
        diag_second - sums[1],
    )


def solution(mesh):
    rows, cols = mesh.devices.shape
    split = jax.sharding.Mesh(mesh.devices.reshape(rows // 2, 2, cols), ("prow_hi", "core", "pcol"))
    prow = ("prow_hi", "core")
    placed = (
        P(None, prow, None, None, "pcol", None),
        P(None, prow, "pcol", None),
        P(None, prow, "pcol", None),
        P(),
        P(),
        P(),
        P(),
    )

    return jax.shard_map(
        body,
        mesh=split,
        in_specs=placed,
        out_specs=(P(None, prow, "pcol", None), P(None, prow, "pcol", None), P(), P()),
        check_vma=False,
    )
```

```python
import jax
import jax.numpy as jnp
from jax import lax
from jax.sharding import PartitionSpec as P


TILE = 128
PIECE = 512


def pack_upper(d):
    n = d.shape[-1] // TILE
    blocks = [
        d[..., i * TILE:(i + 1) * TILE, j * TILE:(j + 1) * TILE]
        for i in range(n)
        for j in range(i, n)
    ]
    return jnp.stack(blocks, axis=-3)


def unpack_upper(packed, n):
    rows = [[None] * n for _ in range(n)]
    k = 0
    for i in range(n):
        for j in range(i, n):
            blk = packed[..., k, :, :]
            rows[i][j] = blk
            if i != j:
                rows[j][i] = jnp.swapaxes(blk, -1, -2)
            k += 1
    return jnp.concatenate([jnp.concatenate(r, axis=-1) for r in rows], axis=-2)


def body(
    inverse_block, panel_first, panel_second, diag_first, diag_second, pattern_first, pattern_second
):
    prow = ("prow_hi", "core")
    row_count = lax.axis_size(prow)
    pair = lax.axis_size("core")
    core = lax.axis_index("core")
    col_count = lax.axis_size("pcol")
    row_index = lax.axis_index(prow)
    col_index = lax.axis_index("pcol")
    row_blocks = inverse_block.shape[0]
    block_rows = inverse_block.shape[2]
    col_blocks = inverse_block.shape[3]
    slice_rows = panel_first.shape[2]
    width = panel_first.shape[3]
    highest = lax.Precision.HIGHEST
    both = ("prow_hi", "core", "pcol")
    swap = [(b, (b + 1) % pair) for b in range(pair)]

    def pair_sum(value, axis):
        split = value.reshape(value.shape[:axis] + (value.shape[axis] // pair, pair) + value.shape[axis + 1:])
        mine = lax.dynamic_index_in_dim(split, core, axis + 1, False)
        other = lax.dynamic_index_in_dim(split, (core + 1) % pair, axis + 1, False)
        return mine + lax.ppermute(other, "core", swap)

    def kept_of(pattern, prow):
        return lax.dynamic_index_in_dim(
            pattern.reshape(row_blocks, row_count), prow, 1, False
        ).astype(jnp.float32)

    own_first = kept_of(pattern_first, row_index)
    own_second = kept_of(pattern_second, row_index)
    x = jnp.concatenate(
        [
            panel_first[:, 0] * own_first[:, None, None],
            panel_second[:, 0] * own_second[:, None, None],
        ],
        axis=-1,
    )

    to_reducer = []
    to_owner = []
    for q in range(row_count):
        for c in range(col_count):
            reducer = (col_count * (q // col_count) + c) * col_count + q % col_count
            to_reducer.append((q * col_count + c, reducer))
            to_owner.append((reducer, q * col_count + c))
    x_at_reducer = lax.ppermute(x, both, to_reducer)

    matrix = inverse_block.reshape(row_blocks, block_rows, col_blocks, block_rows)

    def reduce_inner(piece, by_permutes):
        gathered = gather_piece(piece, by_permutes)
        return reduce_gathered(piece, gathered)

    def gather_piece(piece, by_permutes):
        if by_permutes:
            held = [None] * col_count
            held[0] = piece
            for k in range(1, col_count):
                held[k] = lax.ppermute(
                    piece, "pcol", [(i, (i + k) % col_count) for i in range(col_count)]
                )
            order = jnp.stack(held, axis=1)
            source = (col_index - jnp.arange(col_count)) % col_count
            slot = jnp.argsort(source)
            gathered = jnp.take(order, slot, axis=1).reshape(row_blocks, block_rows, piece.shape[-1])
        else:
            spread = jnp.broadcast_to(
                piece[:, None], (row_blocks, col_count) + piece.shape[1:]
            ).reshape(row_blocks, block_rows, piece.shape[-1])
            gathered = lax.all_to_all(spread, "pcol", 1, 1, tiled=True)
        return gathered

    def reduce_gathered(piece, gathered):
        partial = product_of(gathered)
        chunks = partial.reshape(row_blocks, row_count, slice_rows, piece.shape[-1])
        pre = pair_sum(chunks, 1)
        received = lax.all_to_all(pre, "prow_hi", 1, 1, tiled=True)
        return jnp.sum(received, axis=1)

    def product_of(gathered):
        return jnp.einsum(
            "lsmt,lsw->mtw",
            matrix,
            gathered,
            precision=highest,
            preferred_element_type=jnp.float32,
        )

    total = jnp.concatenate(
        [
            reduce_inner(x[..., k * PIECE:(k + 1) * PIECE], k > 0)
            for k in range(2 * width // PIECE)
        ],
        axis=-1,
    )

    owner_row = col_index + col_count * (row_index // col_count)
    kept_first = kept_of(pattern_first, owner_row)
    kept_second = kept_of(pattern_second, owner_row)
    column = jnp.concatenate(
        [
            -(total[..., :width] * kept_first[:, None, None]),
            -(total[..., width:] * kept_second[:, None, None]),
        ],
        axis=-1,
    )
    parts = jnp.stack(
        [
            jnp.einsum(
                "lsw,lsv->wv",
                x_at_reducer[..., :width],
                column[..., :width],
                precision=highest,
                preferred_element_type=jnp.float32,
            ),
            jnp.einsum(
                "lsw,lsv->wv",
                x_at_reducer[..., width:],
                column[..., width:],
                precision=highest,
                preferred_element_type=jnp.float32,
            ),
        ]
    )
    column_home = lax.ppermute(column, both, to_owner)
    packed = pack_upper(parts)
    others = ("prow_hi", "pcol")
    devices = lax.axis_size(others)
    half = pair_sum(packed.reshape(pair * devices, packed.size // (pair * devices)), 0)
    flat = half.reshape(devices, half.size // devices)
    reduced = jnp.sum(lax.all_to_all(flat, others, 0, 0, tiled=True), axis=0)
    spread_sum = jnp.broadcast_to(reduced[None], flat.shape)
    mine = lax.all_to_all(spread_sum, others, 0, 0, tiled=True).reshape(half.shape)
    other = lax.ppermute(mine, "core", swap)
    summed = jnp.where(
        core == 0,
        jnp.stack([mine, other], axis=1),
        jnp.stack([other, mine], axis=1),
    ).reshape(packed.shape)
    sums = unpack_upper(summed, width // TILE)
    return (
        column_home[:, None, :, :width],
        column_home[:, None, :, width:],
        diag_first - sums[0],
        diag_second - sums[1],
    )


def solution(mesh):
    rows, cols = mesh.devices.shape
    split = jax.sharding.Mesh(mesh.devices.reshape(rows // 2, 2, cols), ("prow_hi", "core", "pcol"))
    prow = ("prow_hi", "core")
    placed = (
        P(None, prow, None, None, "pcol", None),
        P(None, prow, "pcol", None),
        P(None, prow, "pcol", None),
        P(),
        P(),
        P(),
        P(),
    )

    return jax.shard_map(
        body,
        mesh=split,
        in_specs=placed,
        out_specs=(P(None, prow, "pcol", None), P(None, prow, "pcol", None), P(), P()),
        check_vma=False,
    )
```

```python
import jax
import jax.numpy as jnp
from jax import lax
from jax.sharding import PartitionSpec as P


TILE = 128
PIECE = 512


def pack_upper(d):
    n = d.shape[-1] // TILE
    blocks = [
        d[..., i * TILE:(i + 1) * TILE, j * TILE:(j + 1) * TILE]
        for i in range(n)
        for j in range(i, n)
    ]
    return jnp.stack(blocks, axis=-3)


def unpack_upper(packed, n):
    rows = [[None] * n for _ in range(n)]
    k = 0
    for i in range(n):
        for j in range(i, n):
            blk = packed[..., k, :, :]
            rows[i][j] = blk
            if i != j:
                rows[j][i] = jnp.swapaxes(blk, -1, -2)
            k += 1
    return jnp.concatenate([jnp.concatenate(r, axis=-1) for r in rows], axis=-2)


def body(
    inverse_block, panel_first, panel_second, diag_first, diag_second, pattern_first, pattern_second
):
    prow = ("prow_hi", "core")
    row_count = lax.axis_size(prow)
    pair = lax.axis_size("core")
    core = lax.axis_index("core")
    col_count = lax.axis_size("pcol")
    row_index = lax.axis_index(prow)
    col_index = lax.axis_index("pcol")
    row_blocks = inverse_block.shape[0]
    block_rows = inverse_block.shape[2]
    col_blocks = inverse_block.shape[3]
    slice_rows = panel_first.shape[2]
    width = panel_first.shape[3]
    highest = lax.Precision.HIGHEST
    both = ("prow_hi", "core", "pcol")
    swap = [(b, (b + 1) % pair) for b in range(pair)]

    def pair_sum(value, axis):
        split = value.reshape(value.shape[:axis] + (value.shape[axis] // pair, pair) + value.shape[axis + 1:])
        mine = lax.dynamic_index_in_dim(split, core, axis + 1, False)
        other = lax.dynamic_index_in_dim(split, (core + 1) % pair, axis + 1, False)
        return mine + lax.ppermute(other, "core", swap)

    def kept_of(pattern, prow):
        return lax.dynamic_index_in_dim(
            pattern.reshape(row_blocks, row_count), prow, 1, False
        ).astype(jnp.float32)

    own_first = kept_of(pattern_first, row_index)
    own_second = kept_of(pattern_second, row_index)
    x = jnp.concatenate(
        [
            panel_first[:, 0] * own_first[:, None, None],
            panel_second[:, 0] * own_second[:, None, None],
        ],
        axis=-1,
    )

    to_reducer = []
    to_owner = []
    for q in range(row_count):
        for c in range(col_count):
            reducer = (col_count * (q // col_count) + c) * col_count + q % col_count
            to_reducer.append((q * col_count + c, reducer))
            to_owner.append((reducer, q * col_count + c))
    x_at_reducer = lax.ppermute(x, both, to_reducer)

    matrix = inverse_block.reshape(row_blocks, block_rows, col_blocks, block_rows)

    def reduce_inner(piece, by_permutes):
        gathered = gather_piece(piece, by_permutes)
        return reduce_gathered(piece, gathered)

    def gather_piece(piece, by_permutes):
        if by_permutes:
            bits = col_count.bit_length() - 1
            order = [1, 0, 2] if bits == 3 else list(range(bits))
            held = piece
            axes = []
            for b in order:
                mine = (col_index >> b) & 1
                got = lax.ppermute(held, "pcol", [(i, i ^ (1 << b)) for i in range(col_count)])
                pos = sum(1 for a in axes if a > b)
                held = jnp.where(
                    mine == 0,
                    jnp.stack([held, got], axis=pos),
                    jnp.stack([got, held], axis=pos),
                )
                axes.insert(pos, b)
            gathered = jnp.moveaxis(
                held.reshape((col_count,) + piece.shape), 0, 1
            ).reshape(row_blocks, block_rows, piece.shape[-1])
        else:
            spread = jnp.broadcast_to(
                piece[:, None], (row_blocks, col_count) + piece.shape[1:]
            ).reshape(row_blocks, block_rows, piece.shape[-1])
            gathered = lax.all_to_all(spread, "pcol", 1, 1, tiled=True)
        return gathered

    def reduce_gathered(piece, gathered):
        partial = product_of(gathered)
        chunks = partial.reshape(row_blocks, row_count, slice_rows, piece.shape[-1])
        pre = pair_sum(chunks, 1)
        received = lax.all_to_all(pre, "prow_hi", 1, 1, tiled=True)
        return jnp.sum(received, axis=1)

    def product_of(gathered):
        return jnp.einsum(
            "lsmt,lsw->mtw",
            matrix,
            gathered,
            precision=highest,
            preferred_element_type=jnp.float32,
        )

    total = jnp.concatenate(
        [
            reduce_inner(x[..., k * PIECE:(k + 1) * PIECE], k > 0)
            for k in range(2 * width // PIECE)
        ],
        axis=-1,
    )

    owner_row = col_index + col_count * (row_index // col_count)
    kept_first = kept_of(pattern_first, owner_row)
    kept_second = kept_of(pattern_second, owner_row)
    column = jnp.concatenate(
        [
            -(total[..., :width] * kept_first[:, None, None]),
            -(total[..., width:] * kept_second[:, None, None]),
        ],
        axis=-1,
    )
    parts = jnp.stack(
        [
            jnp.einsum(
                "lsw,lsv->wv",
                x_at_reducer[..., :width],
                column[..., :width],
                precision=highest,
                preferred_element_type=jnp.float32,
            ),
            jnp.einsum(
                "lsw,lsv->wv",
                x_at_reducer[..., width:],
                column[..., width:],
                precision=highest,
                preferred_element_type=jnp.float32,
            ),
        ]
    )
    column_home = lax.ppermute(column, both, to_owner)
    packed = pack_upper(parts)
    others = ("prow_hi", "pcol")
    devices = lax.axis_size(others)
    half = pair_sum(packed.reshape(pair * devices, packed.size // (pair * devices)), 0)
    flat = half.reshape(devices, half.size // devices)
    reduced = jnp.sum(lax.all_to_all(flat, others, 0, 0, tiled=True), axis=0)
    spread_sum = jnp.broadcast_to(reduced[None], flat.shape)
    mine = lax.all_to_all(spread_sum, others, 0, 0, tiled=True).reshape(half.shape)
    other = lax.ppermute(mine, "core", swap)
    summed = jnp.where(
        core == 0,
        jnp.stack([mine, other], axis=1),
        jnp.stack([other, mine], axis=1),
    ).reshape(packed.shape)
    sums = unpack_upper(summed, width // TILE)
    return (
        column_home[:, None, :, :width],
        column_home[:, None, :, width:],
        diag_first - sums[0],
        diag_second - sums[1],
    )


def solution(mesh):
    rows, cols = mesh.devices.shape
    split = jax.sharding.Mesh(mesh.devices.reshape(rows // 2, 2, cols), ("prow_hi", "core", "pcol"))
    prow = ("prow_hi", "core")
    placed = (
        P(None, prow, None, None, "pcol", None),
        P(None, prow, "pcol", None),
        P(None, prow, "pcol", None),
        P(),
        P(),
        P(),
        P(),
    )

    return jax.shard_map(
        body,
        mesh=split,
        in_specs=placed,
        out_specs=(P(None, prow, "pcol", None), P(None, prow, "pcol", None), P(), P()),
        check_vma=False,
    )
```

```python
import jax
import jax.numpy as jnp
from jax import lax
from jax.sharding import PartitionSpec as P


TILE = 128
PIECE = 512


def pack_upper(d):
    n = d.shape[-1] // TILE
    blocks = [
        d[..., i * TILE:(i + 1) * TILE, j * TILE:(j + 1) * TILE]
        for i in range(n)
        for j in range(i, n)
    ]
    return jnp.stack(blocks, axis=-3)


def unpack_upper(packed, n):
    rows = [[None] * n for _ in range(n)]
    k = 0
    for i in range(n):
        for j in range(i, n):
            blk = packed[..., k, :, :]
            rows[i][j] = blk
            if i != j:
                rows[j][i] = jnp.swapaxes(blk, -1, -2)
            k += 1
    return jnp.concatenate([jnp.concatenate(r, axis=-1) for r in rows], axis=-2)


def body(
    inverse_block, panel_first, panel_second, diag_first, diag_second, pattern_first, pattern_second
):
    prow = ("prow_hi", "core")
    row_count = lax.axis_size(prow)
    pair = lax.axis_size("core")
    core = lax.axis_index("core")
    col_count = lax.axis_size("pcol")
    row_index = lax.axis_index(prow)
    col_index = lax.axis_index("pcol")
    row_blocks = inverse_block.shape[0]
    block_rows = inverse_block.shape[2]
    col_blocks = inverse_block.shape[3]
    slice_rows = panel_first.shape[2]
    width = panel_first.shape[3]
    highest = lax.Precision.HIGHEST
    both = ("prow_hi", "core", "pcol")
    swap = [(b, (b + 1) % pair) for b in range(pair)]

    def pair_sum(value, axis):
        split = value.reshape(value.shape[:axis] + (value.shape[axis] // pair, pair) + value.shape[axis + 1:])
        mine = lax.dynamic_index_in_dim(split, core, axis + 1, False)
        other = lax.dynamic_index_in_dim(split, (core + 1) % pair, axis + 1, False)
        return mine + lax.ppermute(other, "core", swap)

    def kept_of(pattern, prow):
        return lax.dynamic_index_in_dim(
            pattern.reshape(row_blocks, row_count), prow, 1, False
        ).astype(jnp.float32)

    own_first = kept_of(pattern_first, row_index)
    own_second = kept_of(pattern_second, row_index)
    x = jnp.concatenate(
        [
            panel_first[:, 0] * own_first[:, None, None],
            panel_second[:, 0] * own_second[:, None, None],
        ],
        axis=-1,
    )

    to_reducer = []
    to_owner = []
    for q in range(row_count):
        for c in range(col_count):
            reducer = (col_count * (q // col_count) + c) * col_count + q % col_count
            to_reducer.append((q * col_count + c, reducer))
            to_owner.append((reducer, q * col_count + c))
    x_at_reducer = lax.ppermute(x, both, to_reducer)

    matrix = inverse_block.reshape(row_blocks, block_rows, col_blocks, block_rows)

    def reduce_inner(piece, by_permutes):
        gathered = gather_piece(piece, by_permutes)
        return reduce_gathered(piece, gathered, by_permutes)

    def gather_piece(piece, by_permutes):
        if by_permutes:
            bits = col_count.bit_length() - 1
            order = [1, 0, 2] if bits == 3 else list(range(bits))
            held = piece
            axes = []
            for b in order:
                mine = (col_index >> b) & 1
                got = lax.ppermute(held, "pcol", [(i, i ^ (1 << b)) for i in range(col_count)])
                pos = sum(1 for a in axes if a > b)
                held = jnp.where(
                    mine == 0,
                    jnp.stack([held, got], axis=pos),
                    jnp.stack([got, held], axis=pos),
                )
                axes.insert(pos, b)
            gathered = jnp.moveaxis(
                held.reshape((col_count,) + piece.shape), 0, 1
            ).reshape(row_blocks, block_rows, piece.shape[-1])
        else:
            spread = jnp.broadcast_to(
                piece[:, None], (row_blocks, col_count) + piece.shape[1:]
            ).reshape(row_blocks, block_rows, piece.shape[-1])
            gathered = lax.all_to_all(spread, "pcol", 1, 1, tiled=True)
        return gathered

    def reduce_gathered(piece, gathered, by_permutes):
        partial = product_of(gathered)
        chunks = partial.reshape(row_blocks, row_count, slice_rows, piece.shape[-1])
        pre = pair_sum(chunks, 1)
        if by_permutes:
            return halve_over_prow(pre)
        received = lax.all_to_all(pre, "prow_hi", 1, 1, tiled=True)
        return jnp.sum(received, axis=1)

    def halve_over_prow(pre):
        size = lax.axis_size("prow_hi")
        bits = size.bit_length() - 1
        me = lax.axis_index("prow_hi")
        held = pre.reshape(pre.shape[:1] + (2,) * bits + pre.shape[2:])
        for b in reversed(range(bits)):
            mine = (me >> b) & 1
            keep = lax.dynamic_index_in_dim(held, mine, 1, False)
            send = lax.dynamic_index_in_dim(held, 1 - mine, 1, False)
            held = keep + lax.ppermute(send, "prow_hi", [(i, i ^ (1 << b)) for i in range(size)])
        return held

    def product_of(gathered):
        return jnp.einsum(
            "lsmt,lsw->mtw",
            matrix,
            gathered,
            precision=highest,
            preferred_element_type=jnp.float32,
        )

    total = jnp.concatenate(
        [reduce_inner(x[..., k * PIECE:(k + 1) * PIECE], k > 0) for k in range(2 * width // PIECE)],
        axis=-1,
    )

    owner_row = col_index + col_count * (row_index // col_count)
    kept_first = kept_of(pattern_first, owner_row)
    kept_second = kept_of(pattern_second, owner_row)
    column = jnp.concatenate(
        [
            -(total[..., :width] * kept_first[:, None, None]),
            -(total[..., width:] * kept_second[:, None, None]),
        ],
        axis=-1,
    )
    parts = jnp.stack(
        [
            jnp.einsum(
                "lsw,lsv->wv",
                x_at_reducer[..., :width],
                column[..., :width],
                precision=highest,
                preferred_element_type=jnp.float32,
            ),
            jnp.einsum(
                "lsw,lsv->wv",
                x_at_reducer[..., width:],
                column[..., width:],
                precision=highest,
                preferred_element_type=jnp.float32,
            ),
        ]
    )
    column_home = lax.ppermute(column, both, to_owner)
    packed = pack_upper(parts)
    others = ("prow_hi", "pcol")
    devices = lax.axis_size(others)
    half = pair_sum(packed.reshape(pair * devices, packed.size // (pair * devices)), 0)
    flat = half.reshape(devices, half.size // devices)
    reduced = jnp.sum(lax.all_to_all(flat, others, 0, 0, tiled=True), axis=0)
    spread_sum = jnp.broadcast_to(reduced[None], flat.shape)
    mine = lax.all_to_all(spread_sum, others, 0, 0, tiled=True).reshape(half.shape)
    other = lax.ppermute(mine, "core", swap)
    summed = jnp.where(
        core == 0,
        jnp.stack([mine, other], axis=1),
        jnp.stack([other, mine], axis=1),
    ).reshape(packed.shape)
    sums = unpack_upper(summed, width // TILE)
    return (
        column_home[:, None, :, :width],
        column_home[:, None, :, width:],
        diag_first - sums[0],
        diag_second - sums[1],
    )


def solution(mesh):
    rows, cols = mesh.devices.shape
    split = jax.sharding.Mesh(mesh.devices.reshape(rows // 2, 2, cols), ("prow_hi", "core", "pcol"))
    prow = ("prow_hi", "core")
    placed = (
        P(None, prow, None, None, "pcol", None),
        P(None, prow, "pcol", None),
        P(None, prow, "pcol", None),
        P(),
        P(),
        P(),
        P(),
    )

    return jax.shard_map(
        body,
        mesh=split,
        in_specs=placed,
        out_specs=(P(None, prow, "pcol", None), P(None, prow, "pcol", None), P(), P()),
        check_vma=False,
    )
```

```python
import jax
import jax.numpy as jnp
from jax import lax
from jax.sharding import PartitionSpec as P


TILE = 128
PIECE = 512


def pack_upper(d):
    n = d.shape[-1] // TILE
    blocks = [
        d[..., i * TILE:(i + 1) * TILE, j * TILE:(j + 1) * TILE]
        for i in range(n)
        for j in range(i, n)
    ]
    return jnp.stack(blocks, axis=-3)


def unpack_upper(packed, n):
    rows = [[None] * n for _ in range(n)]
    k = 0
    for i in range(n):
        for j in range(i, n):
            blk = packed[..., k, :, :]
            rows[i][j] = blk
            if i != j:
                rows[j][i] = jnp.swapaxes(blk, -1, -2)
            k += 1
    return jnp.concatenate([jnp.concatenate(r, axis=-1) for r in rows], axis=-2)


def body(
    inverse_block, panel_first, panel_second, diag_first, diag_second, pattern_first, pattern_second
):
    prow = ("prow_hi", "core")
    row_count = lax.axis_size(prow)
    pair = lax.axis_size("core")
    core = lax.axis_index("core")
    col_count = lax.axis_size("pcol")
    row_index = lax.axis_index(prow)
    col_index = lax.axis_index("pcol")
    row_blocks = inverse_block.shape[0]
    block_rows = inverse_block.shape[2]
    col_blocks = inverse_block.shape[3]
    slice_rows = panel_first.shape[2]
    width = panel_first.shape[3]
    highest = lax.Precision.HIGHEST
    both = ("prow_hi", "core", "pcol")
    swap = [(b, (b + 1) % pair) for b in range(pair)]

    def pair_sum(value, axis):
        split = value.reshape(value.shape[:axis] + (value.shape[axis] // pair, pair) + value.shape[axis + 1:])
        mine = lax.dynamic_index_in_dim(split, core, axis + 1, False)
        other = lax.dynamic_index_in_dim(split, (core + 1) % pair, axis + 1, False)
        return mine + lax.ppermute(other, "core", swap)

    def kept_of(pattern, prow):
        return lax.dynamic_index_in_dim(
            pattern.reshape(row_blocks, row_count), prow, 1, False
        ).astype(jnp.float32)

    own_first = kept_of(pattern_first, row_index)
    own_second = kept_of(pattern_second, row_index)
    x = jnp.concatenate(
        [
            panel_first[:, 0] * own_first[:, None, None],
            panel_second[:, 0] * own_second[:, None, None],
        ],
        axis=-1,
    )

    to_reducer = []
    to_owner = []
    for q in range(row_count):
        for c in range(col_count):
            reducer = (col_count * (q // col_count) + c) * col_count + q % col_count
            to_reducer.append((q * col_count + c, reducer))
            to_owner.append((reducer, q * col_count + c))
    x_at_reducer = lax.ppermute(x, both, to_reducer)

    matrix = inverse_block.reshape(row_blocks, block_rows, col_blocks, block_rows)

    def reduce_inner(piece, by_permutes):
        gathered = gather_piece(piece, by_permutes)
        return reduce_gathered(piece, gathered)

    def gather_piece(piece, by_permutes):
        if by_permutes:
            bits = col_count.bit_length() - 1
            order = [1, 0, 2] if bits == 3 else list(range(bits))
            held = piece
            axes = []
            for b in order:
                mine = (col_index >> b) & 1
                got = lax.ppermute(held, "pcol", [(i, i ^ (1 << b)) for i in range(col_count)])
                pos = sum(1 for a in axes if a > b)
                held = jnp.where(
                    mine == 0,
                    jnp.stack([held, got], axis=pos),
                    jnp.stack([got, held], axis=pos),
                )
                axes.insert(pos, b)
            gathered = jnp.moveaxis(
                held.reshape((col_count,) + piece.shape), 0, 1
            ).reshape(row_blocks, block_rows, piece.shape[-1])
        else:
            spread = jnp.broadcast_to(
                piece[:, None], (row_blocks, col_count) + piece.shape[1:]
            ).reshape(row_blocks, block_rows, piece.shape[-1])
            gathered = lax.all_to_all(spread, "pcol", 1, 1, tiled=True)
        return gathered

    def reduce_gathered(piece, gathered):
        partial = product_of(gathered)
        chunks = partial.reshape(row_blocks, row_count, slice_rows, piece.shape[-1])
        pre = pair_sum(chunks, 1)
        received = lax.all_to_all(pre, "prow_hi", 1, 1, tiled=True)
        return jnp.sum(received, axis=1)

    def product_of(gathered):
        return jnp.einsum(
            "lsmt,lsw->mtw",
            matrix,
            gathered,
            precision=highest,
            preferred_element_type=jnp.float32,
        )

    total = jnp.concatenate(
        [reduce_inner(x[..., k * PIECE:(k + 1) * PIECE], k > 0) for k in range(2 * width // PIECE)],
        axis=-1,
    )

    def second_part(a, b):
        return jnp.einsum(
            "lsw,lsv->wv", a, b, precision=highest, preferred_element_type=jnp.float32
        )

    owner_row = col_index + col_count * (row_index // col_count)
    kept_first = kept_of(pattern_first, owner_row)
    kept_second = kept_of(pattern_second, owner_row)
    column = jnp.concatenate(
        [
            -(total[..., :width] * kept_first[:, None, None]),
            -(total[..., width:] * kept_second[:, None, None]),
        ],
        axis=-1,
    )
    parts = jnp.stack(
        [
            jnp.einsum(
                "lsw,lsv->wv",
                x_at_reducer[..., :width],
                column[..., :width],
                precision=highest,
                preferred_element_type=jnp.float32,
            ),
            second_part(
                x_at_reducer[..., width:],
                column[..., width:],
            ),
        ]
    )
    column_home = lax.ppermute(column, both, to_owner)
    packed = pack_upper(parts)
    others = ("prow_hi", "pcol")
    devices = lax.axis_size(others)
    half = pair_sum(packed.reshape(pair * devices, packed.size // (pair * devices)), 0)
    flat = half.reshape(devices, half.size // devices)
    reduced = jnp.sum(lax.all_to_all(flat, others, 0, 0, tiled=True), axis=0)
    spread_sum = jnp.broadcast_to(reduced[None], flat.shape)
    mine = lax.all_to_all(spread_sum, others, 0, 0, tiled=True).reshape(half.shape)
    other = lax.ppermute(mine, "core", swap)
    summed = jnp.where(
        core == 0,
        jnp.stack([mine, other], axis=1),
        jnp.stack([other, mine], axis=1),
    ).reshape(packed.shape)
    sums = unpack_upper(summed, width // TILE)
    return (
        column_home[:, None, :, :width],
        column_home[:, None, :, width:],
        diag_first - sums[0],
        diag_second - sums[1],
    )


def solution(mesh):
    rows, cols = mesh.devices.shape
    split = jax.sharding.Mesh(mesh.devices.reshape(rows // 2, 2, cols), ("prow_hi", "core", "pcol"))
    prow = ("prow_hi", "core")
    placed = (
        P(None, prow, None, None, "pcol", None),
        P(None, prow, "pcol", None),
        P(None, prow, "pcol", None),
        P(),
        P(),
        P(),
        P(),
    )

    return jax.shard_map(
        body,
        mesh=split,
        in_specs=placed,
        out_specs=(P(None, prow, "pcol", None), P(None, prow, "pcol", None), P(), P()),
        check_vma=False,
    )
```
